512 devices in a mesh: section: 32 (over z, x), neuron: 16 (over y, core).
Axes of the slice: x: 4, y: 8, z: 8, core: 2. Of those that a mesh axis runs over, the one named last changes fastest.
Arguments:
- inputs: bfloat16 [6, 32768], P(None, 'neuron'), may hold values from 0 to 2
- weight_tiles: bfloat16 [32, 2048, 128, 128], P('section', 'neuron'), may hold values from -0.07324219 to 0.07910156
- source_block: int32 [32, 2048], P('section', 'neuron'), may hold values from 0 to 255
- target_block: int32 [32, 2048], P('section', 'neuron'), may hold values from 0 to 15
- live_slots: int32 [32, 16], P('section', 'neuron'), may hold values from 16 to 128, as said below
Outputs:
- activations: bfloat16 [32, 6, 32768], P('section', None, 'neuron')
The draws below stay inside these ranges and needn't reach their ends.
Inputs may be any that keep to these rules, and one draw needn't show every extreme that they name: live_slots[l, n] is 128, 64, 32 or 16, and in every layer some shard has all 128 slots live.
All inputs are finite; a program needn't handle non-finite values.
Results may differ from the reference program's by a relative error of at most 0.0045.
Values may be sent and summed in bfloat16 or wider, within the bound.
No kernel may reach another device: no remote copies, remote signals or barrier semaphores. Data moves between devices by JAX's collectives and lax.ppermute only.
A program may use at most 64 MiB of HBM per device.

```python
import jax
import jax.numpy as jnp
from jax import lax

NEURONS = 32768
BLOCK = 128
LAYERS = 32
NBLK = 256
COLS_DEV = 16
SLOTS = 128
SLOT_ALL = 2048
ROWS = 6
N_NEURON = 16


def draw_live_slots(key, part):
    shift_key, pick_key = jax.random.split(key)
    shifts = jax.random.randint(shift_key, (LAYERS, N_NEURON), 0, 4)
    chosen = jax.random.randint(pick_key, (LAYERS, 1), 0, N_NEURON)
    shifts = jnp.where(jnp.arange(N_NEURON)[None, :] == chosen, 0, shifts)
    return jnp.right_shift(jnp.full((LAYERS, N_NEURON), SLOTS, jnp.int32), shifts.astype(jnp.int32)).astype(jnp.int32)


def plant(values, stream_key, low, high):
    shape = values.shape
    spot = [jax.random.randint(jax.random.fold_in(stream_key, axis), (), 0, shape[axis]) for axis in range(len(shape))]
    values = values.at[tuple(spot)].set(low)
    longest = shape.index(max(shape))
    spot[longest] = (spot[longest] + 1) % shape[longest]
    return values.at[tuple(spot)].set(high)


def levels(rng, extent, cuts, smallest, top_value):
    def one(axis_at, blocks):
        heights = jax.random.uniform(jax.random.fold_in(jax.random.fold_in(rng, 6), axis_at), (blocks,), jnp.float32, smallest / len(cuts), top_value / len(cuts))
        return jnp.repeat(jnp.exp(heights), extent[axis_at] // blocks).reshape((-1,) + (1,) * (len(extent) - axis_at - 1))

    factor_of = one(*cuts[0])
    for cut in cuts[1:]:
        factor_of = factor_of * one(*cut)
    return factor_of


def setup_inputs(seed: int = 0) -> dict:
    streams_of = jax.random.split(jax.random.key(seed), 6)
    return {
        "inputs": jnp.clip(2.0 * jax.random.uniform(streams_of[0], (ROWS, NEURONS), jnp.float32) ** levels(streams_of[0], (ROWS, NEURONS), ((1, 16),), -0.2, 0.2), 0.0, 2.0).astype(jnp.bfloat16),
        "weight_tiles": jnp.clip(-0.07324219 + 0.15234375 * jax.random.uniform(streams_of[1], (LAYERS, SLOT_ALL, BLOCK, BLOCK), jnp.float32) ** levels(streams_of[1], (LAYERS, SLOT_ALL, BLOCK, BLOCK), ((0, 32), (1, 16)), -0.2, 0.2), -0.07324219, 0.07910156).astype(jnp.bfloat16),
        "source_block": plant(jax.random.randint(streams_of[2], (LAYERS, SLOT_ALL), 0, NBLK), jax.random.fold_in(streams_of[2], 1), 0, NBLK - 1).astype(jnp.int32),
        "target_block": plant(jax.random.randint(streams_of[3], (LAYERS, SLOT_ALL), 0, COLS_DEV), jax.random.fold_in(streams_of[3], 1), 0, COLS_DEV - 1).astype(jnp.int32),
        "live_slots": draw_live_slots(jax.random.fold_in(streams_of[5], 71), 0),
    }


NEURON_BIAS = -0.3
CLIP_LEVEL = 32.0


def reference(inputs, weight_tiles, source_block, target_block, live_slots):
    block_count = NEURONS // BLOCK
    row_count = inputs.shape[0]
    slot_index = jnp.arange(SLOT_ALL, dtype=jnp.int32)
    shard_of = (slot_index // SLOTS).astype(jnp.int32)
    layer_list = []
    current = inputs
    for layer_num in range(LAYERS):
        shaped = current.reshape(row_count, block_count, BLOCK).astype(jnp.float32)
        picked = jnp.take(shaped, source_block[layer_num], axis=1)
        live_mask = (slot_index - shard_of * SLOTS) < live_slots[layer_num][shard_of]
        partial_value = jnp.einsum("rsk,skj->rsj", picked, weight_tiles[layer_num].astype(jnp.float32), precision=lax.Precision.HIGHEST)
        partial_value = partial_value * live_mask.astype(jnp.float32)[None, :, None]
        target = (shard_of * COLS_DEV + target_block[layer_num]).astype(jnp.int32)
        summed = jnp.zeros((row_count, block_count, BLOCK), jnp.float32).at[:, target, :].add(partial_value)
        current = jnp.clip(summed + NEURON_BIAS, 0.0, CLIP_LEVEL).astype(jnp.bfloat16).reshape(row_count, NEURONS)
        layer_list.append(current)
    return jnp.stack(layer_list)
```

```python
import jax
import jax.numpy as jnp
from jax import lax
from jax.sharding import PartitionSpec as P


NEURON_BIAS = -0.3
CLIP_LEVEL = 32.0


def relay(piece, shift):
    sections = lax.axis_size("section")
    neurons = lax.axis_size("neuron")
    received = []
    for k in range(neurons):
        if shift == 0 and k == 0:
            received.append(piece)
            continue
        route = []
        for s in range(sections):
            if not 0 <= s + shift < sections:
                continue
            for n in range(neurons):
                route.append((s * neurons + n, (s + shift) * neurons + (n + k) % neurons))
        received.append(lax.ppermute(piece, ("section", "neuron"), route))
    return jnp.stack(received)


def layer_apply(pieces, weight_tiles, source_block, target_block, live_slots, neuron_pos):
    neurons, row_count, shard_width = pieces.shape
    slot_count = weight_tiles.shape[1]
    block_size = weight_tiles.shape[2]
    column_count = shard_width // block_size
    source = source_block[0]
    piece_of = (neuron_pos - source // column_count) % neurons
    split = pieces.reshape(neurons, row_count, column_count, block_size)
    picked = split[piece_of, :, source % column_count, :]
    partial_value = jnp.einsum(
        "smk,skj->msj", picked, weight_tiles[0], preferred_element_type=jnp.float32
    )
    live_mask = jnp.arange(slot_count, dtype=jnp.int32) < live_slots[0, 0]
    selector = (
        target_block[0][:, None] == jnp.arange(column_count, dtype=jnp.int32)[None, :]
    ) & live_mask[:, None]
    summed = jnp.einsum(
        "msj,sc->mcj", partial_value, selector.astype(jnp.float32), precision=lax.Precision.HIGHEST
    )
    result = jnp.clip(summed + NEURON_BIAS, 0.0, CLIP_LEVEL).astype(jnp.bfloat16)
    return result.reshape(row_count, column_count * block_size)


def local(inputs, weight_tiles, source_block, target_block, live_slots):
    section_pos = lax.axis_index("section")
    neuron_pos = lax.axis_index("neuron")
    section_count = lax.axis_size("section")
    row_count, shard_width = inputs.shape

    def compute(pieces):
        return layer_apply(pieces, weight_tiles, source_block, target_block, live_slots, neuron_pos)

    def empty(pieces):
        return jnp.zeros((row_count, shard_width), jnp.bfloat16)

    def advance(step_num, state_pair):
        pieces, collected = state_pair
        active = section_pos == step_num
        result = lax.cond(active, compute, empty, pieces)
        collected = jnp.where(active, result, collected)
        return (relay(result, 1), collected)

    pieces = relay(inputs, 0)
    collected = jnp.zeros((row_count, shard_width), jnp.bfloat16)
    pieces, collected = lax.fori_loop(0, section_count - 1, advance, (pieces, collected))
    last = section_pos == section_count - 1
    result = lax.cond(last, compute, empty, pieces)
    collected = jnp.where(last, result, collected)
    return collected[None]


def solution(mesh):
    in_specs = (
        P(None, "neuron"),
        P("section", "neuron", None, None),
        P("section", "neuron"),
        P("section", "neuron"),
        P("section", "neuron"),
    )
    out_specs = P("section", None, "neuron")
    return jax.shard_map(local, mesh=mesh, in_specs=in_specs, out_specs=out_specs, check_vma=False)
```

```python
import jax
import jax.numpy as jnp
from jax import lax
from jax.sharding import PartitionSpec as P

NEURON_BIAS = -0.3
CLIP_LEVEL = 32.0
UNROLL = True


def layer_apply(gathered, weight_tiles, source, selector):
    row_count = gathered.shape[0]
    block_size = weight_tiles.shape[2]
    column_count = selector.shape[1]
    block_count = gathered.shape[1] // block_size
    shaped = gathered.reshape(row_count, block_count, block_size)
    picked = shaped.at[:, source].get(mode="promise_in_bounds")
    partial_value = jnp.einsum(
        "msk,skj->msj", picked, weight_tiles[0], preferred_element_type=jnp.float32
    )
    summed = jnp.einsum(
        "msj,sc->mcj", partial_value, selector, precision=lax.Precision.HIGHEST
    )
    result = jnp.clip(summed + NEURON_BIAS, 0.0, CLIP_LEVEL).astype(jnp.bfloat16)
    return result.reshape(row_count, column_count * block_size)


def local(inputs, weight_tiles, source_block, target_block, live_slots):
    section_pos = lax.axis_index("section")
    section_count = lax.axis_size("section")
    row_count, shard_width = inputs.shape
    slot_count = weight_tiles.shape[1]
    column_count = shard_width // weight_tiles.shape[2]

    source = source_block[0]
    live_mask = jnp.arange(slot_count, dtype=jnp.int32) < live_slots[0, 0]
    selector = (
        (target_block[0][:, None] == jnp.arange(column_count, dtype=jnp.int32)[None, :])
        & live_mask[:, None]
    ).astype(jnp.float32)

    def compute(gathered):
        return layer_apply(gathered, weight_tiles, source, selector)

    def empty(gathered):
        return jnp.zeros((row_count, shard_width), jnp.bfloat16)

    def step(step_num, current, collected, route):
        gathered = lax.all_gather(current, "neuron", axis=1, tiled=True)
        active = section_pos == step_num
        result = lax.cond(active, compute, empty, gathered)
        collected = jnp.where(active, result, collected)
        if route is None:
            return result, collected
        return lax.ppermute(result, "section", route), collected

    collected = jnp.zeros((row_count, shard_width), jnp.bfloat16)
    current = inputs
    if UNROLL:
        for t in range(section_count - 1):
            current, collected = step(t, current, collected, [(t, t + 1)])
    else:
        route = [(i, i + 1) for i in range(section_count - 1)]
        current, collected = lax.fori_loop(
            0, section_count - 1, lambda t, c: step(t, c[0], c[1], route), (current, collected)
        )
    _, collected = step(section_count - 1, current, collected, None)
    return collected[None]


def solution(mesh):
    in_specs = (
        P(None, "neuron"),
        P("section", "neuron", None, None),
        P("section", "neuron"),
        P("section", "neuron"),
        P("section", "neuron"),
    )
    out_specs = P("section", None, "neuron")
    return jax.shard_map(local, mesh=mesh, in_specs=in_specs, out_specs=out_specs, check_vma=False)
```

```python
import jax
import jax.numpy as jnp
from jax import lax
from jax.sharding import PartitionSpec as P

NEURON_BIAS = -0.3
CLIP_LEVEL = 32.0
UNROLL = True


def layer_apply(gathered, weight_tiles, source, selector):
    row_count = gathered.shape[0]
    block_size = weight_tiles.shape[2]
    column_count = selector.shape[1]
    block_count = gathered.shape[1] // block_size
    shaped = gathered.reshape(row_count, block_count, block_size)
    picked = shaped.at[:, source].get(mode="promise_in_bounds")
    partial_value = jnp.einsum(
        "msk,skj->msj", picked, weight_tiles[0], preferred_element_type=jnp.float32
    )
    summed = jnp.einsum(
        "msj,sc->mcj", partial_value, selector, precision=lax.Precision.HIGHEST
    )
    result = jnp.clip(summed + NEURON_BIAS, 0.0, CLIP_LEVEL).astype(jnp.bfloat16)
    return result.reshape(row_count, column_count * block_size)


def local(inputs, weight_tiles, source_block, target_block, live_slots):
    section_pos = lax.axis_index("section")
    section_count = lax.axis_size("section")
    row_count, shard_width = inputs.shape
    slot_count = weight_tiles.shape[1]
    column_count = shard_width // weight_tiles.shape[2]

    source = source_block[0]
    live_mask = jnp.arange(slot_count, dtype=jnp.int32) < live_slots[0, 0]
    selector = (
        (target_block[0][:, None] == jnp.arange(column_count, dtype=jnp.int32)[None, :])
        & live_mask[:, None]
    ).astype(jnp.float32)

    def compute(gathered):
        return layer_apply(gathered, weight_tiles, source, selector)

    def empty(gathered):
        return jnp.zeros((row_count, shard_width), jnp.bfloat16)

    def step(step_num, current, collected, route):
        gathered = lax.all_gather(current, "neuron", axis=1, tiled=True)
        active = section_pos == step_num
        result = compute(gathered)
        collected = jnp.where(active, result, collected)
        if route is None:
            return result, collected
        return lax.ppermute(result, "section", route), collected

    collected = jnp.zeros((row_count, shard_width), jnp.bfloat16)
    current = inputs
    if UNROLL:
        for t in range(section_count - 1):
            current, collected = step(t, current, collected, [(t, t + 1)])
    else:
        route = [(i, i + 1) for i in range(section_count - 1)]
        current, collected = lax.fori_loop(
            0, section_count - 1, lambda t, c: step(t, c[0], c[1], route), (current, collected)
        )
    _, collected = step(section_count - 1, current, collected, None)
    return collected[None]


def solution(mesh):
    in_specs = (
        P(None, "neuron"),
        P("section", "neuron", None, None),
        P("section", "neuron"),
        P("section", "neuron"),
        P("section", "neuron"),
    )
    out_specs = P("section", None, "neuron")
    return jax.shard_map(local, mesh=mesh, in_specs=in_specs, out_specs=out_specs, check_vma=False)
```
